256 devices in a mesh: row: 16 (over x, z_lo), col: 16 (over y, z_hi, core).
Axes of the slice: x: 4, y: 4, z: 8 (z_hi: 2, z_lo: 4; z = z_hi * 4 + z_lo), core: 2. Of those that a mesh axis runs over, the one named last changes fastest.
Arguments:
- hidden: bfloat16 [2560, 8192], P('row', 'col'), may hold values from -6 to 6
- w_query: bfloat16 [8192, 8192], P('col', 'row'), may hold values from -0.0625 to 0.0625
- w_keyval: bfloat16 [8192, 2048], P('col', 'row'), may hold values from -0.15625 to 0.15625
- prefix_cache: bfloat16 [2, 16384, 2048], P(None, 'col', 'row'), may hold values from -60 to 60, as said below
- suffix_lengths: int32 [16], replicated, may hold values from 32 to 160, as said below
- group_ids: int32 [16], replicated, may hold values from 0 to 1, as said below
Outputs:
- attended: bfloat16 [2560, 8192], P('col', 'row')
The draws below stay inside these ranges and needn't reach their ends.
Inputs may be any that keep to these rules, and one draw needn't show every extreme that they name: `suffix_lengths`: every suffix has 32 to 160 live tokens; some request has exactly 160 and some exactly 32. `group_ids`: exactly 8 requests read each prefix. `prefix_cache`: finite values.
All inputs are finite; a program needn't handle non-finite values.
Results may differ from the reference program's by a relative error of at most 0.011.
Values may be sent and summed in bfloat16 or wider, within the bound.
No kernel may reach another device: no remote copies, remote signals or barrier semaphores. Data moves between devices by JAX's collectives and lax.ppermute only.
A program may use at most 128 MiB of HBM per device.

```python
import jax
import jax.numpy as jnp
from jax import lax

D = 8192
HQ = 64
KVH = 8
HD = 128
PREFIX = 16384
SUF = 160
MIN_SUF = 32
GROUPS = 2
REQ_G = 8
REQ = 16
TOK = 2560


def draw_suffix_lengths(key, part):
    values = jax.random.randint(jax.random.fold_in(key, 3), (REQ,), MIN_SUF, SUF + 1)
    order = jax.random.permutation(jax.random.fold_in(key, 11), REQ)
    values = jnp.where(order == 0, SUF, jnp.where(order == 1, MIN_SUF, values))
    return values.astype(jnp.int32)


def draw_group_ids(key, part):
    order = jax.random.permutation(jax.random.fold_in(key, 5), REQ)
    return (order >= REQ_G).astype(jnp.int32)


def draw_prefix_cache(key, part):
    width = 2 * KVH * HD
    base = 2.5 * jax.random.normal(jax.random.fold_in(key, 7), (GROUPS, PREFIX, width), jnp.float32)
    base = jnp.clip(base, -15.0, 15.0)
    return base.astype(jnp.bfloat16)


def block_levels(key, extent, pieces, smallest, top_value):
    gain = 1.0
    for dim, parts in pieces:
        heights = jax.random.uniform(jax.random.fold_in(jax.random.fold_in(key, 6), dim), (parts,), jnp.float32, smallest / len(pieces), top_value / len(pieces))
        gain = gain * jnp.repeat(jnp.exp(heights), extent[dim] // parts).reshape((-1,) + (1,) * (len(extent) - 1 - dim))
    return gain


def gaussian(own_key, extent, spread, limit, pieces=(), kind=jnp.bfloat16):
    gain = block_levels(own_key, extent, pieces, -0.22, 0.18) if pieces else 1.0
    entries = jax.random.normal(own_key, extent, jnp.float32) * spread * gain
    return jnp.minimum(jnp.maximum(entries, -limit), limit).astype(kind)


def setup_inputs(seed: int = 0) -> dict:
    key_of = jax.random.split(jax.random.key(seed), 7)
    return {
        "hidden": gaussian(key_of[0], (TOK, D), 1.0, 6.0, ((0, 16), (1, 16))),
        "w_query": gaussian(key_of[1], (D, HQ * HD), D ** -0.5, 0.0625, ((0, 16), (1, 16))),
        "w_keyval": gaussian(key_of[2], (D, 2 * KVH * HD), (D // 6) ** -0.5, 0.15625, ((0, 16), (1, 16))),
        "prefix_cache": draw_prefix_cache(jax.random.fold_in(key_of[6], 71), 0),
        "suffix_lengths": draw_suffix_lengths(jax.random.fold_in(key_of[6], 71), 0),
        "group_ids": draw_group_ids(jax.random.fold_in(key_of[6], 71), 0),
    }


def rotary_tables(positions):
    freqs = 500000.0 ** (-(jnp.arange(HD // 2, dtype=jnp.float32) * 2.0 / HD))
    angles = positions.astype(jnp.float32)[:, None] * freqs[None, :]
    return jnp.cos(angles), jnp.sin(angles)


def rotate(values, cosine, sine):
    first = values[..., : HD // 2]
    second = values[..., HD // 2:]
    cosine = cosine[:, None, :]
    sine = sine[:, None, :]
    return jnp.concatenate([first * cosine - second * sine, second * cosine + first * sine], axis=-1)


def reference(hidden, w_query, w_keyval, prefix_cache, suffix_lengths, group_ids):
    slots = hidden.shape[0]
    positions = PREFIX + jnp.arange(slots, dtype=jnp.int32) % SUF
    cosine, sine = rotary_tables(positions)
    query = jnp.dot(hidden, w_query, preferred_element_type=jnp.float32).reshape(slots, HQ, HD)
    query = rotate(query, cosine, sine).astype(jnp.bfloat16)
    keyval = jnp.dot(hidden, w_keyval, preferred_element_type=jnp.float32).reshape(slots, KVH, 2, HD)
    suffix_keys = rotate(keyval[:, :, 0], cosine, sine).astype(jnp.bfloat16)
    suffix_values = keyval[:, :, 1].astype(jnp.bfloat16)
    cache = prefix_cache.reshape(GROUPS, PREFIX, KVH, 2, HD)
    group_size = HQ // KVH
    query = query.reshape(REQ, SUF, KVH, group_size, HD)
    suffix_keys = suffix_keys.reshape(REQ, SUF, KVH, HD)
    suffix_values = suffix_values.reshape(REQ, SUF, KVH, HD)
    scale = 1.0 / (HD ** 0.5)

    def per_request(inputs_one):
        req_query, req_keys, req_values, group, length = inputs_one
        chosen = lax.dynamic_index_in_dim(cache, group, 0, keepdims=False)
        places = jnp.arange(SUF, dtype=jnp.int32)
        own_mask = (places[None, :] <= places[:, None]) & (places[None, :] < length)
        full_mask = jnp.concatenate([jnp.ones((SUF, PREFIX), dtype=bool), own_mask], axis=1)

        def per_head(head):
            head_query = lax.dynamic_index_in_dim(req_query, head, 1, keepdims=False)
            head_cache = lax.dynamic_index_in_dim(chosen, head, 1, keepdims=False)
            all_keys = jnp.concatenate([head_cache[:, 0], lax.dynamic_index_in_dim(req_keys, head, 1, keepdims=False)], axis=0)
            all_values = jnp.concatenate([head_cache[:, 1], lax.dynamic_index_in_dim(req_values, head, 1, keepdims=False)], axis=0)
            scores = jnp.einsum("tgd,kd->gtk", head_query.astype(jnp.float32), all_keys.astype(jnp.float32)) * scale
            scores = jnp.where(full_mask[None], scores, -1e30)
            top = jnp.max(scores, axis=-1, keepdims=True)
            weights = jnp.exp(scores - top)
            total = jnp.sum(weights, axis=-1)
            rounded = lax.optimization_barrier(weights.astype(jnp.bfloat16))
            accum = jnp.einsum("gtk,kd->gtd", rounded.astype(jnp.float32), all_values.astype(jnp.float32))
            return accum / total[..., None]

        result = lax.map(per_head, jnp.arange(KVH, dtype=jnp.int32))
        result = jnp.transpose(result, (2, 0, 1, 3))
        live = (places < length).astype(jnp.float32)
        result = result * live[:, None, None, None]
        return result.reshape(SUF, HQ * HD)

    output = lax.map(per_request, (query, suffix_keys, suffix_values, group_ids, suffix_lengths))
    return output.reshape(slots, HQ * HD).astype(jnp.bfloat16)
```

```python
import jax
import jax.numpy as jnp
from jax import lax
from jax.sharding import PartitionSpec as P

HD = 128
PREFIX = 16384
SUF = 160


def partner(value, axis, stride):
    mask = 2**stride
    pairs = [(source, source ^ mask) for source in range(lax.axis_size(axis))]
    return lax.ppermute(value, axis, pairs)


def rotary_tables(positions):
    freqs = 500000.0 ** (-(jnp.arange(HD // 2, dtype=jnp.float32) * 2.0 / HD))
    angles = positions.astype(jnp.float32)[:, None] * freqs[None, :]
    return (jnp.cos(angles), jnp.sin(angles))


def rotate(values, cosine, sine):
    first = values[..., : HD // 2]
    second = values[..., HD // 2 :]
    cosine = cosine[:, None, :]
    sine = sine[:, None, :]
    return jnp.concatenate(
        [first * cosine - second * sine, second * cosine + first * sine], axis=-1
    )


def block_size(count):
    size = count
    for _ in range(24):
        if size > 2048 and size % 2 == 0:
            size = size // 2
    return size


def block_stats(req_query, keys, values, scale):
    scores = jnp.einsum("thd,kd->htk", req_query, keys, preferred_element_type=jnp.float32) * scale
    top = jnp.max(scores, axis=-1)
    weights = jnp.exp(scores - top[..., None])
    total = jnp.sum(weights, axis=-1)
    accum = jnp.einsum(
        "htk,kd->htd", weights.astype(jnp.bfloat16), values, preferred_element_type=jnp.float32
    )
    return (top, total, accum)


def combine(first, second):
    top = jnp.maximum(first[0], second[0])
    scale_one = jnp.exp(first[0] - top)
    scale_two = jnp.exp(second[0] - top)
    total = first[1] * scale_one + second[1] * scale_two
    accum = first[2] * scale_one[..., None] + second[2] * scale_two[..., None]
    return (top, total, accum)


def empty_state(heads_here):
    return (
        jnp.full((heads_here, SUF), -1e30, jnp.float32),
        jnp.zeros((heads_here, SUF), jnp.float32),
        jnp.zeros((heads_here, SUF, HD), jnp.float32),
    )


def attend_keys(req_query, keys, values, scale):
    count = keys.shape[0]
    size = block_size(count)
    key_blocks = keys.reshape(count // size, size, HD)
    value_blocks = values.reshape(count // size, size, HD)

    def advance(state, pieces):
        return (combine(state, block_stats(req_query, pieces[0], pieces[1], scale)), None)

    state, _ = lax.scan(advance, empty_state(req_query.shape[1]), (key_blocks, value_blocks))
    return state


def flat_perm(n_row, n_col, target):
    pairs = []
    for r in range(n_row):
        for c in range(n_col):
            dest = target(r, c)
            if dest is not None:
                pairs.append((r * n_col + c, dest[0] * n_col + dest[1]))
    return pairs


def combine_all(states):
    top = states[0][0]
    for state in states[1:]:
        top = jnp.maximum(top, state[0])
    total = 0.0
    accum = 0.0
    for state in states:
        factor = jnp.exp(state[0] - top)
        total = total + state[1] * factor
        accum = accum + state[2] * factor[..., None]
    return (top, total, accum)


def per_device(hidden, w_query, w_keyval, prefix_cache, suffix_lengths, group_ids):
    n_row = lax.axis_size("row")
    n_col = lax.axis_size("col")
    row_id = lax.axis_index("row")
    col_id = lax.axis_index("col")
    heads_here = w_query.shape[1] // HD
    segments = w_keyval.shape[1] // HD
    scale = 1.0 / HD**0.5
    gathered = lax.all_gather(hidden, "row", axis=0, tiled=True)
    weights_all = jnp.concatenate([w_query, w_keyval], axis=1)
    tok_block = gathered.shape[0] // n_col
    projected = lax.psum_scatter(
        jnp.dot(gathered, weights_all, preferred_element_type=jnp.float32),
        "col",
        scatter_dimension=0,
        tiled=True,
    )
    positions = PREFIX + jnp.arange(tok_block, dtype=jnp.int32) % SUF
    cosine, sine = rotary_tables(positions)
    query = projected[:, : heads_here * HD].reshape(tok_block, heads_here, HD)
    query = rotate(query, cosine, sine).astype(jnp.bfloat16)
    keyval = projected[:, heads_here * HD :].reshape(tok_block, segments, HD)
    segment_ids = row_id * segments + jnp.arange(segments, dtype=jnp.int32)
    is_key = segment_ids % 2 == 0
    keyval = jnp.where(is_key[None, :, None], rotate(keyval, cosine, sine), keyval).astype(
        jnp.bfloat16
    )
    odd = row_id % 2
    is_even = odd == 0
    other_keyval, other_cache = partner((keyval, prefix_cache), "row", 0)
    suffix_keys = jnp.where(is_even, keyval[:, 0], other_keyval[:, 0])
    suffix_values = jnp.where(is_even, other_keyval[:, 0], keyval[:, 0])
    cache_keys = jnp.where(is_even, prefix_cache, other_cache)
    cache_values = jnp.where(is_even, other_cache, prefix_cache)
    kv_block = jnp.concatenate([cache_keys, cache_values], axis=-1)

    half_bit = 2
    handled = col_id ^ (half_bit * odd)
    masks = [m for m in range(1, n_col) if m & half_bit == 0]
    blocks = [lax.dynamic_index_in_dim(kv_block, group_ids[handled], 0, keepdims=False)]
    for mask in masks:
        peer_group = group_ids[(col_id ^ mask) ^ (half_bit * odd)]
        piece = lax.dynamic_index_in_dim(kv_block, peer_group, 0, keepdims=False)
        pairs = [(c, c ^ mask) for c in range(n_col)]
        blocks.append(lax.ppermute(piece, "col", pairs))
    half_kv = jnp.concatenate(blocks, axis=0)
    half_keys = half_kv[:, :HD]
    half_values = half_kv[:, HD:]

    axes = ("row", "col")
    cross = flat_perm(n_row, n_col, lambda r, c: (r ^ 1, c ^ half_bit) if r % 2 == 0 else (r ^ 1, c))
    back = flat_perm(n_row, n_col, lambda r, c: (r ^ 1, c) if r % 2 == 0 else (r ^ 1, c ^ half_bit))
    same = flat_perm(n_row, n_col, lambda r, c: (r, c ^ half_bit) if r % 2 == 1 else None)
    q_cross = lax.ppermute(query, axes, cross)
    q_same = lax.ppermute(query, axes, same)
    q_first = jnp.where(is_even, query, q_cross)
    q_second = jnp.where(is_even, q_cross, q_same)
    q_all = jnp.concatenate([q_first, q_second], axis=1)

    half_state = attend_keys(q_all, half_keys, half_values, scale)
    mine = jax.tree.map(
        lambda a, b: jnp.where(is_even, a, b),
        jax.tree.map(lambda x: x[:heads_here], half_state),
        jax.tree.map(lambda x: x[heads_here:], half_state),
    )
    theirs = jax.tree.map(
        lambda a, b: jnp.where(is_even, a, b),
        jax.tree.map(lambda x: x[heads_here:], half_state),
        jax.tree.map(lambda x: x[:heads_here], half_state),
    )
    from_cross = lax.ppermute(theirs, axes, back)
    from_same = lax.ppermute(mine, axes, same)
    first_state = jax.tree.map(lambda a, b: jnp.where(is_even, a, b), mine, from_same)

    length = suffix_lengths[col_id]
    places = jnp.arange(SUF, dtype=jnp.int32)
    mask = (places[None, :] <= places[:, None]) & (places[None, :] < length)
    scores = (
        jnp.einsum("thd,kd->htk", query, suffix_keys, preferred_element_type=jnp.float32) * scale
    )
    scores = jnp.where(mask[None], scores, -1e30)
    own_top = jnp.max(scores, axis=-1)
    weights = jnp.exp(scores - own_top[..., None])
    own_total = jnp.sum(weights, axis=-1)
    own_accum = jnp.einsum(
        "htk,kd->htd", weights.astype(jnp.bfloat16), suffix_values, preferred_element_type=jnp.float32
    )
    merged = combine_all([first_state, from_cross, (own_top, own_total, own_accum)])
    result = merged[2] / merged[1][..., None]
    live = (places < length).astype(jnp.float32)
    result = result * live[None, :, None]
    return jnp.transpose(result, (1, 0, 2)).reshape(tok_block, heads_here * HD).astype(jnp.bfloat16)


def solution(mesh):
    return jax.shard_map(
        per_device,
        mesh=mesh,
        in_specs=(
            P("row", "col"),
            P("col", "row"),
            P("col", "row"),
            P(None, "col", "row"),
            P(),
            P(),
        ),
        out_specs=P("col", "row"),
        check_vma=False,
    )
```

```python
import jax
import jax.numpy as jnp
from jax import lax
from jax.sharding import PartitionSpec as P

HD = 128
PREFIX = 16384
SUF = 160


def partner(value, axis, stride):
    mask = 2**stride
    pairs = [(source, source ^ mask) for source in range(lax.axis_size(axis))]
    return lax.ppermute(value, axis, pairs)


def rotary_tables(positions):
    freqs = 500000.0 ** (-(jnp.arange(HD // 2, dtype=jnp.float32) * 2.0 / HD))
    angles = positions.astype(jnp.float32)[:, None] * freqs[None, :]
    return (jnp.cos(angles), jnp.sin(angles))


def rotate(values, cosine, sine):
    first = values[..., : HD // 2]
    second = values[..., HD // 2 :]
    cosine = cosine[:, None, :]
    sine = sine[:, None, :]
    return jnp.concatenate(
        [first * cosine - second * sine, second * cosine + first * sine], axis=-1
    )


def block_size(count):
    size = count
    for _ in range(24):
        if size > 2048 and size % 2 == 0:
            size = size // 2
    return size


def block_stats(req_query, keys, values, scale):
    scores = jnp.einsum("thd,kd->htk", req_query, keys, preferred_element_type=jnp.float32) * scale
    top = jnp.max(scores, axis=-1)
    weights = jnp.exp(scores - top[..., None])
    total = jnp.sum(weights, axis=-1)
    accum = jnp.einsum(
        "htk,kd->htd", weights.astype(jnp.bfloat16), values, preferred_element_type=jnp.float32
    )
    return (top, total, accum)


def combine(first, second):
    top = jnp.maximum(first[0], second[0])
    scale_one = jnp.exp(first[0] - top)
    scale_two = jnp.exp(second[0] - top)
    total = first[1] * scale_one + second[1] * scale_two
    accum = first[2] * scale_one[..., None] + second[2] * scale_two[..., None]
    return (top, total, accum)


def empty_state(heads_here):
    return (
        jnp.full((heads_here, SUF), -1e30, jnp.float32),
        jnp.zeros((heads_here, SUF), jnp.float32),
        jnp.zeros((heads_here, SUF, HD), jnp.float32),
    )


def attend_keys(req_query, keys, values, scale):
    count = keys.shape[0]
    size = block_size(count)
    key_blocks = keys.reshape(count // size, size, HD)
    value_blocks = values.reshape(count // size, size, HD)

    def advance(state, pieces):
        return (combine(state, block_stats(req_query, pieces[0], pieces[1], scale)), None)

    state, _ = lax.scan(advance, empty_state(req_query.shape[1]), (key_blocks, value_blocks))
    return state


def flat_perm(n_row, n_col, target):
    pairs = []
    for r in range(n_row):
        for c in range(n_col):
            dest = target(r, c)
            if dest is not None:
                pairs.append((r * n_col + c, dest[0] * n_col + dest[1]))
    return pairs


def combine_all(states):
    top = states[0][0]
    for state in states[1:]:
        top = jnp.maximum(top, state[0])
    total = 0.0
    accum = 0.0
    for state in states:
        factor = jnp.exp(state[0] - top)
        total = total + state[1] * factor
        accum = accum + state[2] * factor[..., None]
    return (top, total, accum)


def per_device(hidden, w_query, w_keyval, prefix_cache, suffix_lengths, group_ids):
    n_row = lax.axis_size("row")
    n_col = lax.axis_size("col")
    row_id = lax.axis_index("row")
    col_id = lax.axis_index("col")
    heads_here = w_query.shape[1] // HD
    segments = w_keyval.shape[1] // HD
    scale = 1.0 / HD**0.5
    half_bit = 2
    stacked = [hidden]
    for mask in range(1, n_row):
        stacked.append(lax.ppermute(hidden, "row", [(i, i ^ mask) for i in range(n_row)]))
    stacked = jnp.stack(stacked)
    order = row_id ^ jnp.arange(n_row, dtype=jnp.int32)
    gathered = jnp.take(stacked, order, axis=0).reshape(-1, hidden.shape[1])
    weights_all = jnp.concatenate([w_query, w_keyval], axis=1)
    tok_block = gathered.shape[0] // n_col
    partial = jnp.dot(gathered, weights_all, preferred_element_type=jnp.float32)
    partial = partial.reshape(n_col, tok_block, partial.shape[1])
    own_pair = jnp.stack(
        [
            lax.dynamic_index_in_dim(partial, col_id, 0, keepdims=False),
            lax.dynamic_index_in_dim(partial, col_id ^ half_bit, 0, keepdims=False),
        ]
    )
    half_sum = own_pair
    low = partial.astype(jnp.bfloat16)
    for mask in [m for m in range(1, n_col) if m & half_bit == 0]:
        peer = col_id ^ mask
        piece = jnp.stack(
            [
                lax.dynamic_index_in_dim(low, peer, 0, keepdims=False),
                lax.dynamic_index_in_dim(low, peer ^ half_bit, 0, keepdims=False),
            ]
        )
        got = lax.ppermute(piece, "col", [(c, c ^ mask) for c in range(n_col)])
        half_sum = half_sum + got.astype(jnp.float32)
    across = lax.ppermute(half_sum[1], "col", [(c, c ^ half_bit) for c in range(n_col)])
    projected = half_sum[0] + across
    positions = PREFIX + jnp.arange(tok_block, dtype=jnp.int32) % SUF
    cosine, sine = rotary_tables(positions)
    query = projected[:, : heads_here * HD].reshape(tok_block, heads_here, HD)
    query = rotate(query, cosine, sine).astype(jnp.bfloat16)
    keyval = projected[:, heads_here * HD :].reshape(tok_block, segments, HD)
    segment_ids = row_id * segments + jnp.arange(segments, dtype=jnp.int32)
    is_key = segment_ids % 2 == 0
    keyval = jnp.where(is_key[None, :, None], rotate(keyval, cosine, sine), keyval).astype(
        jnp.bfloat16
    )
    odd = row_id % 2
    is_even = odd == 0
    other_keyval, other_cache = partner((keyval, prefix_cache), "row", 0)
    suffix_keys = jnp.where(is_even, keyval[:, 0], other_keyval[:, 0])
    suffix_values = jnp.where(is_even, other_keyval[:, 0], keyval[:, 0])
    cache_keys = jnp.where(is_even, prefix_cache, other_cache)
    cache_values = jnp.where(is_even, other_cache, prefix_cache)
    kv_block = jnp.concatenate([cache_keys, cache_values], axis=-1)

    handled = col_id ^ (half_bit * odd)
    masks = [m for m in range(1, n_col) if m & half_bit == 0]
    blocks = [lax.dynamic_index_in_dim(kv_block, group_ids[handled], 0, keepdims=False)]
    for mask in masks:
        peer_group = group_ids[(col_id ^ mask) ^ (half_bit * odd)]
        piece = lax.dynamic_index_in_dim(kv_block, peer_group, 0, keepdims=False)
        pairs = [(c, c ^ mask) for c in range(n_col)]
        blocks.append(lax.ppermute(piece, "col", pairs))
    half_kv = jnp.concatenate(blocks, axis=0)
    half_keys = half_kv[:, :HD]
    half_values = half_kv[:, HD:]

    axes = ("row", "col")
    cross = flat_perm(n_row, n_col, lambda r, c: (r ^ 1, c ^ half_bit) if r % 2 == 0 else (r ^ 1, c))
    back = flat_perm(n_row, n_col, lambda r, c: (r ^ 1, c) if r % 2 == 0 else (r ^ 1, c ^ half_bit))
    same = flat_perm(n_row, n_col, lambda r, c: (r, c ^ half_bit) if r % 2 == 1 else None)
    q_cross = lax.ppermute(query, axes, cross)
    q_same = lax.ppermute(query, axes, same)
    q_first = jnp.where(is_even, query, q_cross)
    q_second = jnp.where(is_even, q_cross, q_same)
    q_all = jnp.concatenate([q_first, q_second], axis=1)

    half_state = attend_keys(q_all, half_keys, half_values, scale)
    mine = jax.tree.map(
        lambda a, b: jnp.where(is_even, a, b),
        jax.tree.map(lambda x: x[:heads_here], half_state),
        jax.tree.map(lambda x: x[heads_here:], half_state),
    )
    theirs = jax.tree.map(
        lambda a, b: jnp.where(is_even, a, b),
        jax.tree.map(lambda x: x[heads_here:], half_state),
        jax.tree.map(lambda x: x[:heads_here], half_state),
    )
    from_cross = lax.ppermute(theirs, axes, back)
    from_same = lax.ppermute(mine, axes, same)
    first_state = jax.tree.map(lambda a, b: jnp.where(is_even, a, b), mine, from_same)

    length = suffix_lengths[col_id]
    places = jnp.arange(SUF, dtype=jnp.int32)
    mask = (places[None, :] <= places[:, None]) & (places[None, :] < length)
    scores = (
        jnp.einsum("thd,kd->htk", query, suffix_keys, preferred_element_type=jnp.float32) * scale
    )
    scores = jnp.where(mask[None], scores, -1e30)
    own_top = jnp.max(scores, axis=-1)
    weights = jnp.exp(scores - own_top[..., None])
    own_total = jnp.sum(weights, axis=-1)
    own_accum = jnp.einsum(
        "htk,kd->htd", weights.astype(jnp.bfloat16), suffix_values, preferred_element_type=jnp.float32
    )
    merged = combine_all([first_state, from_cross, (own_top, own_total, own_accum)])
    result = merged[2] / merged[1][..., None]
    live = (places < length).astype(jnp.float32)
    result = result * live[None, :, None]
    return jnp.transpose(result, (1, 0, 2)).reshape(tok_block, heads_here * HD).astype(jnp.bfloat16)


def solution(mesh):
    return jax.shard_map(
        per_device,
        mesh=mesh,
        in_specs=(
            P("row", "col"),
            P("col", "row"),
            P("col", "row"),
            P(None, "col", "row"),
            P(),
            P(),
        ),
        out_specs=P("col", "row"),
        check_vma=False,
    )
```

```python
import jax
import jax.numpy as jnp
from jax import lax
from jax.sharding import PartitionSpec as P

HD = 128
PREFIX = 16384
SUF = 160


def partner(value, axis, stride):
    mask = 2**stride
    pairs = [(source, source ^ mask) for source in range(lax.axis_size(axis))]
    return lax.ppermute(value, axis, pairs)


def rotary_tables(positions):
    freqs = 500000.0 ** (-(jnp.arange(HD // 2, dtype=jnp.float32) * 2.0 / HD))
    angles = positions.astype(jnp.float32)[:, None] * freqs[None, :]
    return (jnp.cos(angles), jnp.sin(angles))


def rotate(values, cosine, sine):
    first = values[..., : HD // 2]
    second = values[..., HD // 2 :]
    cosine = cosine[:, None, :]
    sine = sine[:, None, :]
    return jnp.concatenate(
        [first * cosine - second * sine, second * cosine + first * sine], axis=-1
    )


def block_size(count):
    size = count
    for _ in range(24):
        if size > 2048 and size % 2 == 0:
            size = size // 2
    return size


def block_stats(req_query, keys, values, scale):
    scores = jnp.einsum("thd,kd->htk", req_query, keys, preferred_element_type=jnp.float32) * scale
    top = jnp.max(scores, axis=-1)
    weights = jnp.exp(scores - top[..., None])
    total = jnp.sum(weights, axis=-1)
    accum = jnp.einsum(
        "htk,kd->htd", weights.astype(jnp.bfloat16), values, preferred_element_type=jnp.float32
    )
    return (top, total, accum)


def combine(first, second):
    top = jnp.maximum(first[0], second[0])
    scale_one = jnp.exp(first[0] - top)
    scale_two = jnp.exp(second[0] - top)
    total = first[1] * scale_one + second[1] * scale_two
    accum = first[2] * scale_one[..., None] + second[2] * scale_two[..., None]
    return (top, total, accum)


def empty_state(heads_here):
    return (
        jnp.full((heads_here, SUF), -1e30, jnp.float32),
        jnp.zeros((heads_here, SUF), jnp.float32),
        jnp.zeros((heads_here, SUF, HD), jnp.float32),
    )


def attend_keys(req_query, keys, values, scale):
    count = keys.shape[0]
    size = block_size(count)
    key_blocks = keys.reshape(count // size, size, HD)
    value_blocks = values.reshape(count // size, size, HD)

    def advance(state, pieces):
        return (combine(state, block_stats(req_query, pieces[0], pieces[1], scale)), None)

    state, _ = lax.scan(advance, empty_state(req_query.shape[1]), (key_blocks, value_blocks))
    return state


def flat_perm(n_row, n_col, target):
    pairs = []
    for r in range(n_row):
        for c in range(n_col):
            dest = target(r, c)
            if dest is not None:
                pairs.append((r * n_col + c, dest[0] * n_col + dest[1]))
    return pairs


def combine_all(states):
    top = states[0][0]
    for state in states[1:]:
        top = jnp.maximum(top, state[0])
    total = 0.0
    accum = 0.0
    for state in states:
        factor = jnp.exp(state[0] - top)
        total = total + state[1] * factor
        accum = accum + state[2] * factor[..., None]
    return (top, total, accum)


def pack_state(state):
    top, total, accum = state
    stats = jnp.stack([top, total]).reshape(-1, HD)
    return jnp.concatenate([accum.reshape(-1, HD), stats], axis=0)


def unpack_state(packed, heads):
    rows = heads * SUF
    accum = packed[:rows].reshape(heads, SUF, HD)
    stats = packed[rows:].reshape(2, heads, SUF)
    return (stats[0], stats[1], accum)


def per_device(hidden, w_query, w_keyval, prefix_cache, suffix_lengths, group_ids):
    n_row = lax.axis_size("row")
    n_col = lax.axis_size("col")
    row_id = lax.axis_index("row")
    col_id = lax.axis_index("col")
    heads_here = w_query.shape[1] // HD
    segments = w_keyval.shape[1] // HD
    scale = 1.0 / HD**0.5
    half_bit = 2
    gathered = lax.all_gather(hidden, "row", axis=0, tiled=True)
    odd = row_id % 2
    is_even = odd == 0
    handled = col_id ^ (half_bit * odd)
    other_cache = partner(prefix_cache, "row", 0)
    cache_keys = jnp.where(is_even, prefix_cache, other_cache)
    cache_values = jnp.where(is_even, other_cache, prefix_cache)
    kv_block = jnp.concatenate([cache_keys, cache_values], axis=-1)

    masks = [m for m in range(1, n_col) if m & half_bit == 0]
    blocks = [lax.dynamic_index_in_dim(kv_block, group_ids[handled], 0, keepdims=False)]
    for mask in masks:
        peer_group = group_ids[(col_id ^ mask) ^ (half_bit * odd)]
        piece = lax.dynamic_index_in_dim(kv_block, peer_group, 0, keepdims=False)
        pairs = [(c, c ^ mask) for c in range(n_col)]
        blocks.append(lax.ppermute(piece, "col", pairs))
    half_kv = jnp.concatenate(blocks, axis=0)
    gathered, half_kv = lax.optimization_barrier((gathered, half_kv))
    weights_all = jnp.concatenate([w_query, w_keyval], axis=1)
    tok_block = gathered.shape[0] // n_col
    partial = jnp.dot(gathered, weights_all, preferred_element_type=jnp.float32)
    partial = partial.reshape(n_col, tok_block, partial.shape[1])
    own_pair = jnp.stack(
        [
            lax.dynamic_index_in_dim(partial, col_id, 0, keepdims=False),
            lax.dynamic_index_in_dim(partial, col_id ^ half_bit, 0, keepdims=False),
        ]
    )
    half_sum = own_pair
    low = partial.astype(jnp.bfloat16)
    for mask in [m for m in range(1, n_col) if m & half_bit == 0]:
        peer = col_id ^ mask
        piece = jnp.stack(
            [
                lax.dynamic_index_in_dim(low, peer, 0, keepdims=False),
                lax.dynamic_index_in_dim(low, peer ^ half_bit, 0, keepdims=False),
            ]
        )
        got = lax.ppermute(piece, "col", [(c, c ^ mask) for c in range(n_col)])
        half_sum = half_sum + got.astype(jnp.float32)
    across = lax.ppermute(half_sum[1], "col", [(c, c ^ half_bit) for c in range(n_col)])
    projected = half_sum[0] + across
    positions = PREFIX + jnp.arange(tok_block, dtype=jnp.int32) % SUF
    cosine, sine = rotary_tables(positions)
    query = projected[:, : heads_here * HD].reshape(tok_block, heads_here, HD)
    query = rotate(query, cosine, sine).astype(jnp.bfloat16)
    keyval = projected[:, heads_here * HD :].reshape(tok_block, segments, HD)
    segment_ids = row_id * segments + jnp.arange(segments, dtype=jnp.int32)
    is_key = segment_ids % 2 == 0
    keyval = jnp.where(is_key[None, :, None], rotate(keyval, cosine, sine), keyval).astype(
        jnp.bfloat16
    )
    other_keyval = partner(keyval, "row", 0)
    suffix_keys = jnp.where(is_even, keyval[:, 0], other_keyval[:, 0])
    suffix_values = jnp.where(is_even, other_keyval[:, 0], keyval[:, 0])
    half_keys = half_kv[:, :HD]
    half_values = half_kv[:, HD:]

    axes = ("row", "col")
    cross = flat_perm(n_row, n_col, lambda r, c: (r ^ 1, c ^ half_bit) if r % 2 == 0 else (r ^ 1, c))
    back = flat_perm(n_row, n_col, lambda r, c: (r ^ 1, c) if r % 2 == 0 else (r ^ 1, c ^ half_bit))
    same = flat_perm(n_row, n_col, lambda r, c: (r, c ^ half_bit) if r % 2 == 1 else None)
    q_cross = lax.ppermute(query, axes, cross)
    q_same = lax.ppermute(query, axes, same)
    q_first = jnp.where(is_even, query, q_cross)
    q_second = jnp.where(is_even, q_cross, q_same)
    q_all = jnp.concatenate([q_first, q_second], axis=1)

    half_state = attend_keys(q_all, half_keys, half_values, scale)
    mine = jax.tree.map(
        lambda a, b: jnp.where(is_even, a, b),
        jax.tree.map(lambda x: x[:heads_here], half_state),
        jax.tree.map(lambda x: x[heads_here:], half_state),
    )
    theirs = jax.tree.map(
        lambda a, b: jnp.where(is_even, a, b),
        jax.tree.map(lambda x: x[heads_here:], half_state),
        jax.tree.map(lambda x: x[:heads_here], half_state),
    )
    from_cross = unpack_state(lax.ppermute(pack_state(theirs), axes, back), heads_here)
    from_same = unpack_state(lax.ppermute(pack_state(mine), axes, same), heads_here)
    first_state = jax.tree.map(lambda a, b: jnp.where(is_even, a, b), mine, from_same)

    length = suffix_lengths[col_id]
    places = jnp.arange(SUF, dtype=jnp.int32)
    mask = (places[None, :] <= places[:, None]) & (places[None, :] < length)
    scores = (
        jnp.einsum("thd,kd->htk", query, suffix_keys, preferred_element_type=jnp.float32) * scale
    )
    scores = jnp.where(mask[None], scores, -1e30)
    own_top = jnp.max(scores, axis=-1)
    weights = jnp.exp(scores - own_top[..., None])
    own_total = jnp.sum(weights, axis=-1)
    own_accum = jnp.einsum(
        "htk,kd->htd", weights.astype(jnp.bfloat16), suffix_values, preferred_element_type=jnp.float32
    )
    merged = combine_all([first_state, from_cross, (own_top, own_total, own_accum)])
    result = merged[2] / merged[1][..., None]
    live = (places < length).astype(jnp.float32)
    result = result * live[None, :, None]
    return jnp.transpose(result, (1, 0, 2)).reshape(tok_block, heads_here * HD).astype(jnp.bfloat16)


def solution(mesh):
    return jax.shard_map(
        per_device,
        mesh=mesh,
        in_specs=(
            P("row", "col"),
            P("col", "row"),
            P("col", "row"),
            P(None, "col", "row"),
            P(),
            P(),
        ),
        out_specs=P("col", "row"),
        check_vma=False,
    )
```

```python
import functools

import jax
import jax.numpy as jnp
from jax import lax
from jax.experimental import pallas as pl
from jax.experimental.pallas import tpu as pltpu
from jax.sharding import PartitionSpec as P

HD = 128
PREFIX = 16384
SUF = 160


def partner(value, axis, stride):
    mask = 2**stride
    pairs = [(source, source ^ mask) for source in range(lax.axis_size(axis))]
    return lax.ppermute(value, axis, pairs)


def rotary_tables(positions):
    freqs = 500000.0 ** (-(jnp.arange(HD // 2, dtype=jnp.float32) * 2.0 / HD))
    angles = positions.astype(jnp.float32)[:, None] * freqs[None, :]
    return (jnp.cos(angles), jnp.sin(angles))


def rotate(values, cosine, sine):
    first = values[..., : HD // 2]
    second = values[..., HD // 2 :]
    cosine = cosine[:, None, :]
    sine = sine[:, None, :]
    return jnp.concatenate(
        [first * cosine - second * sine, second * cosine + first * sine], axis=-1
    )


def block_size(count):
    size = count
    for _ in range(24):
        if size > 2048 and size % 2 == 0:
            size = size // 2
    return size


def block_stats(req_query, keys, values, scale):
    scores = jnp.einsum("thd,kd->htk", req_query, keys, preferred_element_type=jnp.float32) * scale
    top = jnp.max(scores, axis=-1)
    weights = jnp.exp(scores - top[..., None])
    total = jnp.sum(weights, axis=-1)
    accum = jnp.einsum(
        "htk,kd->htd", weights.astype(jnp.bfloat16), values, preferred_element_type=jnp.float32
    )
    return (top, total, accum)


def combine(first, second):
    top = jnp.maximum(first[0], second[0])
    scale_one = jnp.exp(first[0] - top)
    scale_two = jnp.exp(second[0] - top)
    total = first[1] * scale_one + second[1] * scale_two
    accum = first[2] * scale_one[..., None] + second[2] * scale_two[..., None]
    return (top, total, accum)


def empty_state(heads_here):
    return (
        jnp.full((heads_here, SUF), -1e30, jnp.float32),
        jnp.zeros((heads_here, SUF), jnp.float32),
        jnp.zeros((heads_here, SUF, HD), jnp.float32),
    )


def attend_keys(req_query, keys, values, scale):
    count = keys.shape[0]
    size = block_size(count)
    key_blocks = keys.reshape(count // size, size, HD)
    value_blocks = values.reshape(count // size, size, HD)

    def advance(state, pieces):
        return (combine(state, block_stats(req_query, pieces[0], pieces[1], scale)), None)

    state, _ = lax.scan(advance, empty_state(req_query.shape[1]), (key_blocks, value_blocks))
    return state


def flash_kernel(scale, q_ref, k_ref, v_ref, acc_ref, top_ref, total_ref):
    step = pl.program_id(0)

    @pl.when(step == 0)
    def _():
        acc_ref[...] = jnp.zeros_like(acc_ref)
        top_ref[...] = jnp.full_like(top_ref, -1e30)
        total_ref[...] = jnp.zeros_like(total_ref)

    scores = lax.dot_general(
        q_ref[...], k_ref[...], (((1,), (1,)), ((), ())), preferred_element_type=jnp.float32
    ) * scale
    old_top = top_ref[...]
    new_top = jnp.maximum(old_top, jnp.max(scores, axis=1, keepdims=True))
    factor = jnp.exp(old_top - new_top)
    weights = jnp.exp(scores - new_top)
    total_ref[...] = total_ref[...] * factor + jnp.sum(weights, axis=1, keepdims=True)
    acc_ref[...] = acc_ref[...] * factor + jnp.dot(
        weights.astype(jnp.bfloat16), v_ref[...], preferred_element_type=jnp.float32
    )
    top_ref[...] = new_top


def prefix_attention(q_rows, joined, scale, block=512):
    rows = q_rows.shape[0]
    count = joined.shape[0]
    cost = pl.CostEstimate(
        flops=4 * rows * count * HD,
        transcendentals=rows * count,
        bytes_accessed=2 * (2 * count * HD + rows * HD) + 4 * rows * (HD + 2),
    )
    acc, top, total = pl.pallas_call(
        functools.partial(flash_kernel, scale),
        grid=(count // block,),
        in_specs=[
            pl.BlockSpec((rows, HD), lambda i: (0, 0)),
            pl.BlockSpec((block, HD), lambda i: (i, 0)),
            pl.BlockSpec((block, HD), lambda i: (i, 1)),
        ],
        out_specs=[
            pl.BlockSpec((rows, HD), lambda i: (0, 0)),
            pl.BlockSpec((rows, 1), lambda i: (0, 0)),
            pl.BlockSpec((rows, 1), lambda i: (0, 0)),
        ],
        out_shape=[
            jax.ShapeDtypeStruct((rows, HD), jnp.float32),
            jax.ShapeDtypeStruct((rows, 1), jnp.float32),
            jax.ShapeDtypeStruct((rows, 1), jnp.float32),
        ],
        compiler_params=pltpu.CompilerParams(dimension_semantics=("arbitrary",)),
        cost_estimate=cost,
    )(q_rows, joined, joined)
    return top[:, 0], total[:, 0], acc


def flat_perm(n_row, n_col, target):
    pairs = []
    for r in range(n_row):
        for c in range(n_col):
            dest = target(r, c)
            if dest is not None:
                pairs.append((r * n_col + c, dest[0] * n_col + dest[1]))
    return pairs


def combine_all(states):
    top = states[0][0]
    for state in states[1:]:
        top = jnp.maximum(top, state[0])
    total = 0.0
    accum = 0.0
    for state in states:
        factor = jnp.exp(state[0] - top)
        total = total + state[1] * factor
        accum = accum + state[2] * factor[..., None]
    return (top, total, accum)


def pack_state(state):
    top, total, accum = state
    stats = jnp.stack([top, total]).reshape(-1, HD)
    return jnp.concatenate([accum.reshape(-1, HD), stats], axis=0)


def unpack_state(packed, heads):
    rows = heads * SUF
    accum = packed[:rows].reshape(heads, SUF, HD)
    stats = packed[rows:].reshape(2, heads, SUF)
    return (stats[0], stats[1], accum)


def per_device(hidden, w_query, w_keyval, prefix_cache, suffix_lengths, group_ids):
    n_row = lax.axis_size("row")
    n_col = lax.axis_size("col")
    row_id = lax.axis_index("row")
    col_id = lax.axis_index("col")
    heads_here = w_query.shape[1] // HD
    segments = w_keyval.shape[1] // HD
    scale = 1.0 / HD**0.5
    half_bit = 2
    gathered = lax.all_gather(hidden, "row", axis=0, tiled=True)
    odd = row_id % 2
    is_even = odd == 0
    handled = col_id ^ (half_bit * odd)
    other_cache = partner(prefix_cache, "row", 0)
    cache_keys = jnp.where(is_even, prefix_cache, other_cache)
    cache_values = jnp.where(is_even, other_cache, prefix_cache)
    kv_block = jnp.concatenate([cache_keys, cache_values], axis=-1)

    masks = [m for m in range(1, n_col) if m & half_bit == 0]
    blocks = [lax.dynamic_index_in_dim(kv_block, group_ids[handled], 0, keepdims=False)]
    for mask in masks:
        peer_group = group_ids[(col_id ^ mask) ^ (half_bit * odd)]
        piece = lax.dynamic_index_in_dim(kv_block, peer_group, 0, keepdims=False)
        pairs = [(c, c ^ mask) for c in range(n_col)]
        blocks.append(lax.ppermute(piece, "col", pairs))
    half_kv = jnp.concatenate(blocks, axis=0)
    gathered, half_kv = lax.optimization_barrier((gathered, half_kv))
    weights_all = jnp.concatenate([w_query, w_keyval], axis=1)
    tok_block = gathered.shape[0] // n_col
    partial = jnp.dot(gathered, weights_all, preferred_element_type=jnp.float32)
    partial = partial.reshape(n_col, tok_block, partial.shape[1])
    own_pair = jnp.stack(
        [
            lax.dynamic_index_in_dim(partial, col_id, 0, keepdims=False),
            lax.dynamic_index_in_dim(partial, col_id ^ half_bit, 0, keepdims=False),
        ]
    )
    half_sum = own_pair
    low = partial.astype(jnp.bfloat16)
    for mask in [m for m in range(1, n_col) if m & half_bit == 0]:
        peer = col_id ^ mask
        piece = jnp.stack(
            [
                lax.dynamic_index_in_dim(low, peer, 0, keepdims=False),
                lax.dynamic_index_in_dim(low, peer ^ half_bit, 0, keepdims=False),
            ]
        )
        got = lax.ppermute(piece, "col", [(c, c ^ mask) for c in range(n_col)])
        half_sum = half_sum + got.astype(jnp.float32)
    across = lax.ppermute(half_sum[1], "col", [(c, c ^ half_bit) for c in range(n_col)])
    projected = half_sum[0] + across
    positions = PREFIX + jnp.arange(tok_block, dtype=jnp.int32) % SUF
    cosine, sine = rotary_tables(positions)
    query = projected[:, : heads_here * HD].reshape(tok_block, heads_here, HD)
    query = rotate(query, cosine, sine).astype(jnp.bfloat16)
    keyval = projected[:, heads_here * HD :].reshape(tok_block, segments, HD)
    segment_ids = row_id * segments + jnp.arange(segments, dtype=jnp.int32)
    is_key = segment_ids % 2 == 0
    keyval = jnp.where(is_key[None, :, None], rotate(keyval, cosine, sine), keyval).astype(
        jnp.bfloat16
    )
    other_keyval = partner(keyval, "row", 0)
    suffix_keys = jnp.where(is_even, keyval[:, 0], other_keyval[:, 0])
    suffix_values = jnp.where(is_even, other_keyval[:, 0], keyval[:, 0])

    axes = ("row", "col")
    cross = flat_perm(n_row, n_col, lambda r, c: (r ^ 1, c ^ half_bit) if r % 2 == 0 else (r ^ 1, c))
    back = flat_perm(n_row, n_col, lambda r, c: (r ^ 1, c) if r % 2 == 0 else (r ^ 1, c ^ half_bit))
    same = flat_perm(n_row, n_col, lambda r, c: (r, c ^ half_bit) if r % 2 == 1 else None)
    q_cross = lax.ppermute(query, axes, cross)
    q_same = lax.ppermute(query, axes, same)
    q_first = jnp.where(is_even, query, q_cross)
    q_second = jnp.where(is_even, q_cross, q_same)
    q_all = jnp.concatenate([q_first, q_second], axis=1)

    heads_all = q_all.shape[1]
    q_rows = jnp.transpose(q_all, (1, 0, 2)).reshape(-1, HD)
    top, total, accum = prefix_attention(q_rows, half_kv, scale)
    half_state = (
        top.reshape(heads_all, SUF),
        total.reshape(heads_all, SUF),
        accum.reshape(heads_all, SUF, HD),
    )
    mine = jax.tree.map(
        lambda a, b: jnp.where(is_even, a, b),
        jax.tree.map(lambda x: x[:heads_here], half_state),
        jax.tree.map(lambda x: x[heads_here:], half_state),
    )
    theirs = jax.tree.map(
        lambda a, b: jnp.where(is_even, a, b),
        jax.tree.map(lambda x: x[heads_here:], half_state),
        jax.tree.map(lambda x: x[:heads_here], half_state),
    )
    from_cross = unpack_state(lax.ppermute(pack_state(theirs), axes, back), heads_here)
    from_same = unpack_state(lax.ppermute(pack_state(mine), axes, same), heads_here)
    first_state = jax.tree.map(lambda a, b: jnp.where(is_even, a, b), mine, from_same)

    length = suffix_lengths[col_id]
    places = jnp.arange(SUF, dtype=jnp.int32)
    mask = (places[None, :] <= places[:, None]) & (places[None, :] < length)
    scores = (
        jnp.einsum("thd,kd->htk", query, suffix_keys, preferred_element_type=jnp.float32) * scale
    )
    scores = jnp.where(mask[None], scores, -1e30)
    own_top = jnp.max(scores, axis=-1)
    weights = jnp.exp(scores - own_top[..., None])
    own_total = jnp.sum(weights, axis=-1)
    own_accum = jnp.einsum(
        "htk,kd->htd", weights.astype(jnp.bfloat16), suffix_values, preferred_element_type=jnp.float32
    )
    merged = combine_all([first_state, from_cross, (own_top, own_total, own_accum)])
    result = merged[2] / merged[1][..., None]
    live = (places < length).astype(jnp.float32)
    result = result * live[None, :, None]
    return jnp.transpose(result, (1, 0, 2)).reshape(tok_block, heads_here * HD).astype(jnp.bfloat16)


def solution(mesh):
    return jax.shard_map(
        per_device,
        mesh=mesh,
        in_specs=(
            P("row", "col"),
            P("col", "row"),
            P("col", "row"),
            P(None, "col", "row"),
            P(),
            P(),
        ),
        out_specs=P("col", "row"),
        check_vma=False,
    )
```

```python
import functools

import jax
import jax.numpy as jnp
from jax import lax
from jax.sharding import Mesh
from jax.sharding import PartitionSpec as P

HD = 128
PREFIX = 16384
SUF = 160
ROW = ("x", "zl")
COL = ("y", "zh", "core")


def partner(value, axis, stride, size):
    mask = 2**stride
    pairs = [(source, source ^ mask) for source in range(size)]
    return lax.ppermute(value, axis, pairs)


def rotary_tables(positions):
    freqs = 500000.0 ** (-(jnp.arange(HD // 2, dtype=jnp.float32) * 2.0 / HD))
    angles = positions.astype(jnp.float32)[:, None] * freqs[None, :]
    return (jnp.cos(angles), jnp.sin(angles))


def rotate(values, cosine, sine):
    first = values[..., : HD // 2]
    second = values[..., HD // 2 :]
    cosine = cosine[:, None, :]
    sine = sine[:, None, :]
    return jnp.concatenate(
        [first * cosine - second * sine, second * cosine + first * sine], axis=-1
    )


def block_size(count):
    size = count
    for _ in range(24):
        if size > 2048 and size % 2 == 0:
            size = size // 2
    return size


def block_stats(req_query, keys, values, scale):
    scores = jnp.einsum("thd,kd->htk", req_query, keys, preferred_element_type=jnp.float32) * scale
    top = jnp.max(scores, axis=-1)
    weights = jnp.exp(scores - top[..., None])
    total = jnp.sum(weights, axis=-1)
    accum = jnp.einsum(
        "htk,kd->htd", weights.astype(jnp.bfloat16), values, preferred_element_type=jnp.float32
    )
    return (top, total, accum)


def combine(first, second):
    top = jnp.maximum(first[0], second[0])
    scale_one = jnp.exp(first[0] - top)
    scale_two = jnp.exp(second[0] - top)
    total = first[1] * scale_one + second[1] * scale_two
    accum = first[2] * scale_one[..., None] + second[2] * scale_two[..., None]
    return (top, total, accum)


def empty_state(heads_here):
    return (
        jnp.full((heads_here, SUF), -1e30, jnp.float32),
        jnp.zeros((heads_here, SUF), jnp.float32),
        jnp.zeros((heads_here, SUF, HD), jnp.float32),
    )


def attend_keys(req_query, keys, values, scale):
    count = keys.shape[0]
    size = block_size(count)
    key_blocks = keys.reshape(count // size, size, HD)
    value_blocks = values.reshape(count // size, size, HD)

    def advance(state, pieces):
        return (combine(state, block_stats(req_query, pieces[0], pieces[1], scale)), None)

    state, _ = lax.scan(advance, empty_state(req_query.shape[1]), (key_blocks, value_blocks))
    return state


def flat_perm(n_row, n_col, target):
    pairs = []
    for r in range(n_row):
        for c in range(n_col):
            dest = target(r, c)
            if dest is not None:
                pairs.append((r * n_col + c, dest[0] * n_col + dest[1]))
    return pairs


def combine_all(states):
    top = states[0][0]
    for state in states[1:]:
        top = jnp.maximum(top, state[0])
    total = 0.0
    accum = 0.0
    for state in states:
        factor = jnp.exp(state[0] - top)
        total = total + state[1] * factor
        accum = accum + state[2] * factor[..., None]
    return (top, total, accum)


def pack_state(state):
    top, total, accum = state
    stats = jnp.stack([top, total]).reshape(-1, HD)
    return jnp.concatenate([accum.reshape(-1, HD), stats], axis=0)


def unpack_state(packed, heads):
    rows = heads * SUF
    accum = packed[:rows].reshape(heads, SUF, HD)
    stats = packed[rows:].reshape(2, heads, SUF)
    return (stats[0], stats[1], accum)


def per_device(n_row, n_col, hidden, w_query, w_keyval, prefix_cache, suffix_lengths, group_ids):
    row_id = lax.axis_index(ROW)
    col_id = lax.axis_index(COL)
    heads_here = w_query.shape[1] // HD
    segments = w_keyval.shape[1] // HD
    scale = 1.0 / HD**0.5
    half_bit = 2
    n_low = n_row // 4
    low_id = lax.axis_index("zl")
    stacked = [hidden]
    for mask in range(1, n_low):
        stacked.append(lax.ppermute(hidden, "zl", [(i, i ^ mask) for i in range(n_low)]))
    stacked = jnp.stack(stacked)
    order = low_id ^ jnp.arange(n_low, dtype=jnp.int32)
    gathered = jnp.take(stacked, order, axis=0).reshape(-1, hidden.shape[1])
    gathered = lax.all_gather(gathered, "x", axis=0, tiled=True)
    odd = row_id % 2
    is_even = odd == 0
    handled = col_id ^ (half_bit * odd)
    other_cache = partner(prefix_cache, ROW, 0, n_row)
    cache_keys = jnp.where(is_even, prefix_cache, other_cache)
    cache_values = jnp.where(is_even, other_cache, prefix_cache)
    kv_block = jnp.concatenate([cache_keys, cache_values], axis=-1)

    masks = [m for m in range(1, n_col) if m & half_bit == 0]
    blocks = [lax.dynamic_index_in_dim(kv_block, group_ids[handled], 0, keepdims=False)]
    for mask in masks:
        peer_group = group_ids[(col_id ^ mask) ^ (half_bit * odd)]
        piece = lax.dynamic_index_in_dim(kv_block, peer_group, 0, keepdims=False)
        pairs = [(c, c ^ mask) for c in range(n_col)]
        blocks.append(lax.ppermute(piece, COL, pairs))
    half_kv = jnp.concatenate(blocks, axis=0)
    gathered, half_kv = lax.optimization_barrier((gathered, half_kv))
    weights_all = jnp.concatenate([w_query, w_keyval], axis=1)
    tok_block = gathered.shape[0] // n_col
    partial = jnp.dot(gathered, weights_all, preferred_element_type=jnp.float32)
    partial = partial.reshape(n_col, tok_block, partial.shape[1])
    own_pair = jnp.stack(
        [
            lax.dynamic_index_in_dim(partial, col_id, 0, keepdims=False),
            lax.dynamic_index_in_dim(partial, col_id ^ half_bit, 0, keepdims=False),
        ]
    )
    half_sum = own_pair
    low = partial.astype(jnp.bfloat16)
    for mask in [m for m in range(1, n_col) if m & half_bit == 0]:
        peer = col_id ^ mask
        piece = jnp.stack(
            [
                lax.dynamic_index_in_dim(low, peer, 0, keepdims=False),
                lax.dynamic_index_in_dim(low, peer ^ half_bit, 0, keepdims=False),
            ]
        )
        got = lax.ppermute(piece, COL, [(c, c ^ mask) for c in range(n_col)])
        half_sum = half_sum + got.astype(jnp.float32)
    across = lax.ppermute(half_sum[1], COL, [(c, c ^ half_bit) for c in range(n_col)])
    projected = half_sum[0] + across
    positions = PREFIX + jnp.arange(tok_block, dtype=jnp.int32) % SUF
    cosine, sine = rotary_tables(positions)
    query = projected[:, : heads_here * HD].reshape(tok_block, heads_here, HD)
    query = rotate(query, cosine, sine).astype(jnp.bfloat16)
    keyval = projected[:, heads_here * HD :].reshape(tok_block, segments, HD)
    segment_ids = row_id * segments + jnp.arange(segments, dtype=jnp.int32)
    is_key = segment_ids % 2 == 0
    keyval = jnp.where(is_key[None, :, None], rotate(keyval, cosine, sine), keyval).astype(
        jnp.bfloat16
    )
    other_keyval = partner(keyval, ROW, 0, n_row)
    suffix_keys = jnp.where(is_even, keyval[:, 0], other_keyval[:, 0])
    suffix_values = jnp.where(is_even, other_keyval[:, 0], keyval[:, 0])
    half_keys = half_kv[:, :HD]
    half_values = half_kv[:, HD:]

    axes = ROW + COL
    cross = flat_perm(n_row, n_col, lambda r, c: (r ^ 1, c ^ half_bit) if r % 2 == 0 else (r ^ 1, c))
    back = flat_perm(n_row, n_col, lambda r, c: (r ^ 1, c) if r % 2 == 0 else (r ^ 1, c ^ half_bit))
    same = flat_perm(n_row, n_col, lambda r, c: (r, c ^ half_bit) if r % 2 == 1 else None)
    q_cross = lax.ppermute(query, axes, cross)
    q_same = lax.ppermute(query, axes, same)
    q_first = jnp.where(is_even, query, q_cross)
    q_second = jnp.where(is_even, q_cross, q_same)
    q_all = jnp.concatenate([q_first, q_second], axis=1)

    half_state = attend_keys(q_all, half_keys, half_values, scale)
    mine = jax.tree.map(
        lambda a, b: jnp.where(is_even, a, b),
        jax.tree.map(lambda x: x[:heads_here], half_state),
        jax.tree.map(lambda x: x[heads_here:], half_state),
    )
    theirs = jax.tree.map(
        lambda a, b: jnp.where(is_even, a, b),
        jax.tree.map(lambda x: x[heads_here:], half_state),
        jax.tree.map(lambda x: x[:heads_here], half_state),
    )
    from_cross = unpack_state(lax.ppermute(pack_state(theirs), axes, back), heads_here)
    from_same = unpack_state(lax.ppermute(pack_state(mine), axes, same), heads_here)
    first_state = jax.tree.map(lambda a, b: jnp.where(is_even, a, b), mine, from_same)

    length = suffix_lengths[col_id]
    places = jnp.arange(SUF, dtype=jnp.int32)
    mask = (places[None, :] <= places[:, None]) & (places[None, :] < length)
    scores = (
        jnp.einsum("thd,kd->htk", query, suffix_keys, preferred_element_type=jnp.float32) * scale
    )
    scores = jnp.where(mask[None], scores, -1e30)
    own_top = jnp.max(scores, axis=-1)
    weights = jnp.exp(scores - own_top[..., None])
    own_total = jnp.sum(weights, axis=-1)
    own_accum = jnp.einsum(
        "htk,kd->htd", weights.astype(jnp.bfloat16), suffix_values, preferred_element_type=jnp.float32
    )
    merged = combine_all([first_state, from_cross, (own_top, own_total, own_accum)])
    result = merged[2] / merged[1][..., None]
    live = (places < length).astype(jnp.float32)
    result = result * live[None, :, None]
    return jnp.transpose(result, (1, 0, 2)).reshape(tok_block, heads_here * HD).astype(jnp.bfloat16)


def solution(mesh):
    n_row, n_col = mesh.devices.shape
    fine = Mesh(mesh.devices.reshape(4, n_row // 4, 4, 2, n_col // 8), ROW + COL)
    return jax.shard_map(
        functools.partial(per_device, n_row, n_col),
        mesh=fine,
        in_specs=(
            P(ROW, COL),
            P(COL, ROW),
            P(COL, ROW),
            P(None, COL, ROW),
            P(),
            P(),
        ),
        out_specs=P(COL, ROW),
        check_vma=False,
    )
```

```python
import functools

import jax
import jax.numpy as jnp
from jax import lax
from jax.sharding import Mesh
from jax.sharding import PartitionSpec as P

HD = 128
PREFIX = 16384
SUF = 160
ROW = ("x", "zl")
COL = ("y", "zh", "core")


def partner(value, axis, stride, size):
    mask = 2**stride
    pairs = [(source, source ^ mask) for source in range(size)]
    return lax.ppermute(value, axis, pairs)


def rotary_tables(positions):
    freqs = 500000.0 ** (-(jnp.arange(HD // 2, dtype=jnp.float32) * 2.0 / HD))
    angles = positions.astype(jnp.float32)[:, None] * freqs[None, :]
    return (jnp.cos(angles), jnp.sin(angles))


def rotate(values, cosine, sine):
    first = values[..., : HD // 2]
    second = values[..., HD // 2 :]
    cosine = cosine[:, None, :]
    sine = sine[:, None, :]
    return jnp.concatenate(
        [first * cosine - second * sine, second * cosine + first * sine], axis=-1
    )


def block_size(count):
    size = count
    for _ in range(24):
        if size > 2048 and size % 2 == 0:
            size = size // 2
    return size


def block_stats(req_query, keys, values, scale):
    scores = jnp.einsum("thd,kd->htk", req_query, keys, preferred_element_type=jnp.float32) * scale
    top = jnp.max(scores, axis=-1)
    weights = jnp.exp(scores - top[..., None])
    total = jnp.sum(weights, axis=-1)
    accum = jnp.einsum(
        "htk,kd->htd", weights.astype(jnp.bfloat16), values, preferred_element_type=jnp.float32
    )
    return (top, total, accum)


def combine(first, second):
    top = jnp.maximum(first[0], second[0])
    scale_one = jnp.exp(first[0] - top)
    scale_two = jnp.exp(second[0] - top)
    total = first[1] * scale_one + second[1] * scale_two
    accum = first[2] * scale_one[..., None] + second[2] * scale_two[..., None]
    return (top, total, accum)


def empty_state(heads_here):
    return (
        jnp.full((heads_here, SUF), -1e30, jnp.float32),
        jnp.zeros((heads_here, SUF), jnp.float32),
        jnp.zeros((heads_here, SUF, HD), jnp.float32),
    )


def attend_keys(req_query, keys, values, scale):
    count = keys.shape[0]
    size = block_size(count)
    key_blocks = keys.reshape(count // size, size, HD)
    value_blocks = values.reshape(count // size, size, HD)

    def advance(state, pieces):
        return (combine(state, block_stats(req_query, pieces[0], pieces[1], scale)), None)

    state, _ = lax.scan(advance, empty_state(req_query.shape[1]), (key_blocks, value_blocks))
    return state


def flat_perm(n_row, n_col, target):
    pairs = []
    for r in range(n_row):
        for c in range(n_col):
            dest = target(r, c)
            if dest is not None:
                pairs.append((r * n_col + c, dest[0] * n_col + dest[1]))
    return pairs


def combine_all(states):
    top = states[0][0]
    for state in states[1:]:
        top = jnp.maximum(top, state[0])
    total = 0.0
    accum = 0.0
    for state in states:
        factor = jnp.exp(state[0] - top)
        total = total + state[1] * factor
        accum = accum + state[2] * factor[..., None]
    return (top, total, accum)


def pack_state(state):
    top, total, accum = state
    stats = jnp.stack([top, total]).reshape(-1, HD)
    return jnp.concatenate([accum.reshape(-1, HD), stats], axis=0)


def unpack_state(packed, heads):
    rows = heads * SUF
    accum = packed[:rows].reshape(heads, SUF, HD)
    stats = packed[rows:].reshape(2, heads, SUF)
    return (stats[0], stats[1], accum)


def per_device(n_row, n_col, hidden, w_query, w_keyval, prefix_cache, suffix_lengths, group_ids):
    row_id = lax.axis_index(ROW)
    col_id = lax.axis_index(COL)
    heads_here = w_query.shape[1] // HD
    segments = w_keyval.shape[1] // HD
    scale = 1.0 / HD**0.5
    half_bit = 2
    other_cache = partner(prefix_cache, ROW, 0, n_row)
    hidden, other_cache = lax.optimization_barrier((hidden, other_cache))
    n_low = n_row // 4
    low_id = lax.axis_index("zl")
    stacked = [hidden]
    for mask in range(1, n_low):
        stacked.append(lax.ppermute(hidden, "zl", [(i, i ^ mask) for i in range(n_low)]))
    stacked = jnp.stack(stacked)
    order = low_id ^ jnp.arange(n_low, dtype=jnp.int32)
    gathered = jnp.take(stacked, order, axis=0).reshape(-1, hidden.shape[1])
    gathered = lax.all_gather(gathered, "x", axis=0, tiled=True)
    odd = row_id % 2
    is_even = odd == 0
    handled = col_id ^ (half_bit * odd)
    cache_keys = jnp.where(is_even, prefix_cache, other_cache)
    cache_values = jnp.where(is_even, other_cache, prefix_cache)
    kv_block = jnp.concatenate([cache_keys, cache_values], axis=-1)

    masks = [m for m in range(1, n_col) if m & half_bit == 0]
    blocks = [lax.dynamic_index_in_dim(kv_block, group_ids[handled], 0, keepdims=False)]
    for mask in masks:
        peer_group = group_ids[(col_id ^ mask) ^ (half_bit * odd)]
        piece = lax.dynamic_index_in_dim(kv_block, peer_group, 0, keepdims=False)
        pairs = [(c, c ^ mask) for c in range(n_col)]
        blocks.append(lax.ppermute(piece, COL, pairs))
    half_kv = jnp.concatenate(blocks, axis=0)
    gathered, half_kv = lax.optimization_barrier((gathered, half_kv))
    weights_all = jnp.concatenate([w_query, w_keyval], axis=1)
    tok_block = gathered.shape[0] // n_col
    partial = jnp.dot(gathered, weights_all, preferred_element_type=jnp.float32)
    partial = partial.reshape(n_col, tok_block, partial.shape[1])
    own_pair = jnp.stack(
        [
            lax.dynamic_index_in_dim(partial, col_id, 0, keepdims=False),
            lax.dynamic_index_in_dim(partial, col_id ^ half_bit, 0, keepdims=False),
        ]
    )
    half_sum = own_pair
    low = partial.astype(jnp.bfloat16)
    for mask in [m for m in range(1, n_col) if m & half_bit == 0]:
        peer = col_id ^ mask
        piece = jnp.stack(
            [
                lax.dynamic_index_in_dim(low, peer, 0, keepdims=False),
                lax.dynamic_index_in_dim(low, peer ^ half_bit, 0, keepdims=False),
            ]
        )
        got = lax.ppermute(piece, COL, [(c, c ^ mask) for c in range(n_col)])
        half_sum = half_sum + got.astype(jnp.float32)
    across = lax.ppermute(half_sum[1], COL, [(c, c ^ half_bit) for c in range(n_col)])
    projected = half_sum[0] + across
    positions = PREFIX + jnp.arange(tok_block, dtype=jnp.int32) % SUF
    cosine, sine = rotary_tables(positions)
    query = projected[:, : heads_here * HD].reshape(tok_block, heads_here, HD)
    query = rotate(query, cosine, sine).astype(jnp.bfloat16)
    keyval = projected[:, heads_here * HD :].reshape(tok_block, segments, HD)
    segment_ids = row_id * segments + jnp.arange(segments, dtype=jnp.int32)
    is_key = segment_ids % 2 == 0
    keyval = jnp.where(is_key[None, :, None], rotate(keyval, cosine, sine), keyval).astype(
        jnp.bfloat16
    )
    other_keyval = partner(keyval, ROW, 0, n_row)
    suffix_keys = jnp.where(is_even, keyval[:, 0], other_keyval[:, 0])
    suffix_values = jnp.where(is_even, other_keyval[:, 0], keyval[:, 0])
    half_keys = half_kv[:, :HD]
    half_values = half_kv[:, HD:]

    axes = ROW + COL
    cross = flat_perm(n_row, n_col, lambda r, c: (r ^ 1, c ^ half_bit) if r % 2 == 0 else (r ^ 1, c))
    back = flat_perm(n_row, n_col, lambda r, c: (r ^ 1, c) if r % 2 == 0 else (r ^ 1, c ^ half_bit))
    same = flat_perm(n_row, n_col, lambda r, c: (r, c ^ half_bit) if r % 2 == 1 else None)
    q_cross = lax.ppermute(query, axes, cross)
    q_same = lax.ppermute(query, axes, same)
    q_first = jnp.where(is_even, query, q_cross)
    q_second = jnp.where(is_even, q_cross, q_same)
    q_all = jnp.concatenate([q_first, q_second], axis=1)

    half_state = attend_keys(q_all, half_keys, half_values, scale)
    mine = jax.tree.map(
        lambda a, b: jnp.where(is_even, a, b),
        jax.tree.map(lambda x: x[:heads_here], half_state),
        jax.tree.map(lambda x: x[heads_here:], half_state),
    )
    theirs = jax.tree.map(
        lambda a, b: jnp.where(is_even, a, b),
        jax.tree.map(lambda x: x[heads_here:], half_state),
        jax.tree.map(lambda x: x[:heads_here], half_state),
    )
    from_cross = unpack_state(lax.ppermute(pack_state(theirs), axes, back), heads_here)
    from_same = unpack_state(lax.ppermute(pack_state(mine), axes, same), heads_here)
    first_state = jax.tree.map(lambda a, b: jnp.where(is_even, a, b), mine, from_same)

    length = suffix_lengths[col_id]
    places = jnp.arange(SUF, dtype=jnp.int32)
    mask = (places[None, :] <= places[:, None]) & (places[None, :] < length)
    scores = (
        jnp.einsum("thd,kd->htk", query, suffix_keys, preferred_element_type=jnp.float32) * scale
    )
    scores = jnp.where(mask[None], scores, -1e30)
    own_top = jnp.max(scores, axis=-1)
    weights = jnp.exp(scores - own_top[..., None])
    own_total = jnp.sum(weights, axis=-1)
    own_accum = jnp.einsum(
        "htk,kd->htd", weights.astype(jnp.bfloat16), suffix_values, preferred_element_type=jnp.float32
    )
    merged = combine_all([first_state, from_cross, (own_top, own_total, own_accum)])
    result = merged[2] / merged[1][..., None]
    live = (places < length).astype(jnp.float32)
    result = result * live[None, :, None]
    return jnp.transpose(result, (1, 0, 2)).reshape(tok_block, heads_here * HD).astype(jnp.bfloat16)


def solution(mesh):
    n_row, n_col = mesh.devices.shape
    fine = Mesh(mesh.devices.reshape(4, n_row // 4, 4, 2, n_col // 8), ROW + COL)
    return jax.shard_map(
        functools.partial(per_device, n_row, n_col),
        mesh=fine,
        in_specs=(
            P(ROW, COL),
            P(COL, ROW),
            P(COL, ROW),
            P(None, COL, ROW),
            P(),
            P(),
        ),
        out_specs=P(COL, ROW),
        check_vma=False,
    )
```

```python
import jax
import jax.numpy as jnp
from jax import lax
from jax.sharding import PartitionSpec as P

HD = 128
PREFIX = 16384
SUF = 160


def partner(value, axis, stride):
    mask = 2**stride
    pairs = [(source, source ^ mask) for source in range(lax.axis_size(axis))]
    return lax.ppermute(value, axis, pairs)


def rotary_tables(positions):
    freqs = 500000.0 ** (-(jnp.arange(HD // 2, dtype=jnp.float32) * 2.0 / HD))
    angles = positions.astype(jnp.float32)[:, None] * freqs[None, :]
    return (jnp.cos(angles), jnp.sin(angles))


def rotate(values, cosine, sine):
    first = values[..., : HD // 2]
    second = values[..., HD // 2 :]
    cosine = cosine[:, None, :]
    sine = sine[:, None, :]
    return jnp.concatenate(
        [first * cosine - second * sine, second * cosine + first * sine], axis=-1
    )


def block_size(count):
    size = count
    for _ in range(24):
        if size > 2048 and size % 2 == 0:
            size = size // 2
    return size


def block_stats(req_query, keys, values, scale):
    scores = jnp.einsum("thd,kd->htk", req_query, keys, preferred_element_type=jnp.float32) * scale
    top = jnp.max(scores, axis=-1)
    weights = jnp.exp(scores - top[..., None])
    total = jnp.sum(weights, axis=-1)
    accum = jnp.einsum(
        "htk,kd->htd", weights.astype(jnp.bfloat16), values, preferred_element_type=jnp.float32
    )
    return (top, total, accum)


def combine(first, second):
    top = jnp.maximum(first[0], second[0])
    scale_one = jnp.exp(first[0] - top)
    scale_two = jnp.exp(second[0] - top)
    total = first[1] * scale_one + second[1] * scale_two
    accum = first[2] * scale_one[..., None] + second[2] * scale_two[..., None]
    return (top, total, accum)


def empty_state(heads_here):
    return (
        jnp.full((heads_here, SUF), -1e30, jnp.float32),
        jnp.zeros((heads_here, SUF), jnp.float32),
        jnp.zeros((heads_here, SUF, HD), jnp.float32),
    )


def attend_keys(req_query, keys, values, scale):
    count = keys.shape[0]
    size = block_size(count)
    key_blocks = keys.reshape(count // size, size, HD)
    value_blocks = values.reshape(count // size, size, HD)

    def advance(state, pieces):
        return (combine(state, block_stats(req_query, pieces[0], pieces[1], scale)), None)

    state, _ = lax.scan(advance, empty_state(req_query.shape[1]), (key_blocks, value_blocks))
    return state


def flat_perm(n_row, n_col, target):
    pairs = []
    for r in range(n_row):
        for c in range(n_col):
            dest = target(r, c)
            if dest is not None:
                pairs.append((r * n_col + c, dest[0] * n_col + dest[1]))
    return pairs


def combine_all(states):
    top = states[0][0]
    for state in states[1:]:
        top = jnp.maximum(top, state[0])
    total = 0.0
    accum = 0.0
    for state in states:
        factor = jnp.exp(state[0] - top)
        total = total + state[1] * factor
        accum = accum + state[2] * factor[..., None]
    return (top, total, accum)


def pack_state(state):
    top, total, accum = state
    stats = jnp.stack([top, total]).reshape(-1, HD)
    return jnp.concatenate([accum.reshape(-1, HD), stats], axis=0)


def unpack_state(packed, heads):
    rows = heads * SUF
    accum = packed[:rows].reshape(heads, SUF, HD)
    stats = packed[rows:].reshape(2, heads, SUF)
    return (stats[0], stats[1], accum)


def per_device(hidden, w_query, w_keyval, prefix_cache, suffix_lengths, group_ids):
    n_row = lax.axis_size("row")
    n_col = lax.axis_size("col")
    row_id = lax.axis_index("row")
    col_id = lax.axis_index("col")
    heads_here = w_query.shape[1] // HD
    segments = w_keyval.shape[1] // HD
    scale = 1.0 / HD**0.5
    half_bit = 2
    gathered = lax.all_gather(hidden, "row", axis=0, tiled=True)
    odd = row_id % 2
    is_even = odd == 0
    handled = col_id ^ (half_bit * odd)
    other_cache = partner(prefix_cache, "row", 0)
    cache_keys = jnp.where(is_even, prefix_cache, other_cache)
    cache_values = jnp.where(is_even, other_cache, prefix_cache)
    kv_block = jnp.concatenate([cache_keys, cache_values], axis=-1)

    masks = [m for m in range(1, n_col) if m & half_bit == 0]
    blocks = [lax.dynamic_index_in_dim(kv_block, group_ids[handled], 0, keepdims=False)]
    for mask in masks:
        peer_group = group_ids[(col_id ^ mask) ^ (half_bit * odd)]
        piece = lax.dynamic_index_in_dim(kv_block, peer_group, 0, keepdims=False)
        pairs = [(c, c ^ mask) for c in range(n_col)]
        blocks.append(lax.ppermute(piece, "col", pairs))
    half_kv = jnp.concatenate(blocks, axis=0)
    gathered, half_kv = lax.optimization_barrier((gathered, half_kv))
    weights_all = jnp.concatenate([w_query, w_keyval], axis=1)
    tok_block = gathered.shape[0] // n_col
    partial = jnp.dot(gathered, weights_all, preferred_element_type=jnp.float32)
    partial = partial.reshape(n_col, tok_block, partial.shape[1])
    own_pair = jnp.stack(
        [
            lax.dynamic_index_in_dim(partial, col_id, 0, keepdims=False),
            lax.dynamic_index_in_dim(partial, col_id ^ half_bit, 0, keepdims=False),
        ]
    )
    half_sum = own_pair
    low = partial.astype(jnp.bfloat16)
    for mask in [m for m in range(1, n_col) if m & half_bit == 0]:
        peer = col_id ^ mask
        piece = jnp.stack(
            [
                lax.dynamic_index_in_dim(low, peer, 0, keepdims=False),
                lax.dynamic_index_in_dim(low, peer ^ half_bit, 0, keepdims=False),
            ]
        )
        got = lax.ppermute(piece, "col", [(c, c ^ mask) for c in range(n_col)])
        half_sum = half_sum + got.astype(jnp.float32)
    kept = jnp.where(is_even, half_sum[0], half_sum[1])
    sent = jnp.where(is_even, half_sum[1], half_sum[0])
    across = lax.ppermute(sent, "col", [(c, c ^ half_bit) for c in range(n_col)])
    projected = kept + across
    positions = PREFIX + jnp.arange(tok_block, dtype=jnp.int32) % SUF
    cosine, sine = rotary_tables(positions)
    query = projected[:, : heads_here * HD].reshape(tok_block, heads_here, HD)
    query = rotate(query, cosine, sine).astype(jnp.bfloat16)
    keyval = projected[:, heads_here * HD :].reshape(tok_block, segments, HD)
    segment_ids = row_id * segments + jnp.arange(segments, dtype=jnp.int32)
    is_key = segment_ids % 2 == 0
    keyval = jnp.where(is_key[None, :, None], rotate(keyval, cosine, sine), keyval).astype(
        jnp.bfloat16
    )
    axes = ("row", "col")
    pair = flat_perm(n_row, n_col, lambda r, c: (r ^ 1, c ^ half_bit))
    back = flat_perm(n_row, n_col, lambda r, c: (r ^ 1, c) if r % 2 == 0 else (r ^ 1, c ^ half_bit))
    same = flat_perm(n_row, n_col, lambda r, c: (r, c ^ half_bit) if r % 2 == 1 else None)
    mixed = jnp.concatenate([query, keyval], axis=1)
    other = lax.ppermute(mixed, axes, pair)
    other_query = other[:, :heads_here]
    other_keyval = other[:, heads_here:]
    q_all = jnp.where(
        is_even,
        jnp.concatenate([query, other_query], axis=1),
        jnp.concatenate([other_query, query], axis=1),
    )
    suffix_keys = jnp.where(is_even, keyval[:, 0], other_keyval[:, 0])
    suffix_values = jnp.where(is_even, other_keyval[:, 0], keyval[:, 0])

    half_keys = half_kv[:, :HD]
    half_values = half_kv[:, HD:]
    half_state = attend_keys(q_all, half_keys, half_values, scale)
    places = jnp.arange(SUF, dtype=jnp.int32)
    handled_length = suffix_lengths[handled]
    own_mask = (places[None, :] <= places[:, None]) & (places[None, :] < handled_length) & is_even
    scores = (
        jnp.einsum("thd,kd->htk", q_all, suffix_keys, preferred_element_type=jnp.float32) * scale
    )
    scores = jnp.where(own_mask[None], scores, -1e30)
    own_top = jnp.maximum(jnp.max(scores, axis=-1), half_state[0])
    weights = jnp.exp(scores - own_top[..., None])
    weights = jnp.where(own_mask[None], weights, 0.0)
    own_total = jnp.sum(weights, axis=-1)
    own_accum = jnp.einsum(
        "htk,kd->htd", weights.astype(jnp.bfloat16), suffix_values, preferred_element_type=jnp.float32
    )
    half_state = combine_all([half_state, (own_top, own_total, own_accum)])
    mine = jax.tree.map(
        lambda a, b: jnp.where(is_even, a, b),
        jax.tree.map(lambda x: x[:heads_here], half_state),
        jax.tree.map(lambda x: x[heads_here:], half_state),
    )
    theirs = jax.tree.map(
        lambda a, b: jnp.where(is_even, a, b),
        jax.tree.map(lambda x: x[heads_here:], half_state),
        jax.tree.map(lambda x: x[:heads_here], half_state),
    )
    from_cross = unpack_state(lax.ppermute(pack_state(theirs), axes, back), heads_here)
    from_same = unpack_state(lax.ppermute(pack_state(mine), axes, same), heads_here)
    first_state = jax.tree.map(lambda a, b: jnp.where(is_even, a, b), mine, from_same)

    length = suffix_lengths[col_id]
    merged = combine_all([first_state, from_cross])
    result = merged[2] / merged[1][..., None]
    live = (places < length).astype(jnp.float32)
    result = result * live[None, :, None]
    return jnp.transpose(result, (1, 0, 2)).reshape(tok_block, heads_here * HD).astype(jnp.bfloat16)


def solution(mesh):
    return jax.shard_map(
        per_device,
        mesh=mesh,
        in_specs=(
            P("row", "col"),
            P("col", "row"),
            P("col", "row"),
            P(None, "col", "row"),
            P(),
            P(),
        ),
        out_specs=P("col", "row"),
        check_vma=False,
    )
```
